32 devices in a mesh: grp: 2 (over y), vec: 8 (over z, x), orb: 2 (over core).
Axes of the slice: x: 2, y: 2, z: 4, core: 2. Of those that a mesh axis runs over, the one named last changes fastest.
Arguments:
- vectors: bfloat16 [32, 1024, 1024], P(('grp', 'vec'), None, 'orb'), parts along dimension 0, may hold values from -6 to 6
- rotation: bfloat16 [2048, 1024], P(('grp', 'vec', 'orb')), parts along dimension 0, may hold values from -0.1875 to 0.1875
- active: int32 [32, 2], P(('grp', 'vec')), parts along dimension 0, may hold values from 0 to 7, all different within a row
- factors: bfloat16 [32, 256, 1024], P(('grp', 'vec'), None, 'orb'), parts along dimension 0, may hold values from -0.09375 to 0.09375
- owner: int32 [16], P('grp'), parts along dimension 0, may hold values from 0 to 7, each once
Outputs:
- fock_owned: float32 [2048, 1024], P(('grp', 'vec'), 'orb'), parts along dimension 0
The draws below stay inside these ranges and needn't reach their ends.
There are 2 independent parts, one for each index of `grp`. The reference program is written for one: setup_inputs(seed, part) draws one part's arguments, and reference() takes and returns one part's arrays. A program takes and returns all parts, laid end to end along the dimension named above; each array names one. Nothing has to cross between parts.
Inputs may be any that keep to these rules, and one draw needn't show every extreme that they name: `active`: each row names 2 different orbital blocks. Each row group has exactly one owner.
All inputs are finite; a program needn't handle non-finite values.
Results may differ from the reference program's by a relative error of at most 0.004.
Values may be sent and summed in bfloat16 or wider, within the bound.
No kernel may reach another device: no remote copies, remote signals or barrier semaphores. Data moves between devices by JAX's collectives and lax.ppermute only.
A program may use at most 64 MiB of HBM per device.

```python
import jax
import jax.numpy as jnp
from jax import lax

N = 1024
B = 128
KA = 2
NB = 8
ACT = 256
NV = 16
GROUPS = 8


def spiked(result, key, source, target, parts, factor):
    def block_of(dim):
        return (jnp.arange(result.shape[dim]) // (result.shape[dim] // parts)).reshape((-1,) + (1,) * (result.ndim - 1 - dim))

    one_side = jax.random.permutation(key, parts)[block_of(target)]
    other_side = (block_of(target) + parts // 2) % parts
    return jnp.where((block_of(source) == one_side) | (block_of(source) == other_side), factor * result, result)


def shard_levels(stream_key, extent, pieces, low, largest):
    level, own = 1.0, jax.random.fold_in(stream_key, 6)
    for dim, shards_of in pieces:
        heights = jnp.exp(jax.random.uniform(jax.random.fold_in(own, dim), (shards_of,), jnp.float32, low / len(pieces), largest / len(pieces)))
        level = level * jnp.repeat(heights, extent[dim] // shards_of).reshape([-1 if axis == dim else 1 for axis in range(len(extent))])
    return level


def picks_of(rng, rows, number_of, top, lift):
    order = jax.random.permutation(jax.random.fold_in(rng, 1), number_of)
    boost = order
    for power in range(3):
        boost = boost * boost // number_of
    boost = boost * lift // number_of
    lots = jax.random.randint(jax.random.fold_in(rng, 2), (rows, number_of), 0, 4096) + boost
    holders = jax.random.permutation(jax.random.fold_in(rng, 3), rows)[jnp.arange(number_of) % rows]
    lots = jnp.where(jnp.arange(rows)[:, None] == holders[None, :], 1 << 14, lots)
    score = lots * number_of + jnp.arange(number_of)
    return lax.top_k(score.astype(jnp.int32), top)[1].astype(jnp.int32)


def normal_values(key, extent, deviation, most, split=(), kind=jnp.bfloat16):
    factor_of = shard_levels(key, extent, split, -0.22, 0.18) if split else 1.0
    result = jax.random.normal(key, extent, jnp.float32) * deviation * factor_of
    return jnp.minimum(jnp.maximum(result, -most), most).astype(kind)


def bell_draw_with(rng, dims, scale, reach, cuts, heavy, held_as=jnp.bfloat16):
    values = scale * jax.random.normal(rng, dims, jnp.float32)
    if cuts:
        values = values * shard_levels(rng, dims, cuts, -0.22, 0.18)
    return jnp.clip(spiked(values, jax.random.fold_in(rng, 3), *heavy), -reach, reach).astype(held_as)


def setup_inputs(seed: int = 0, part: int = 0) -> dict:
    arg_keys = jax.random.split(jax.random.key(seed), 6)
    part_keys = jax.random.split(jax.random.fold_in(arg_keys[5], part), 6)
    vectors = bell_draw_with(part_keys[0], (NV, N, N), 1.0, 6.0, ((0, 8), (2, 2)), (0, 1, 8, 2.0))
    rotation = normal_values(part_keys[1], (N, N), N ** -0.5, 0.1875, ((0, 16),))
    active = picks_of(part_keys[2], NV, NB, KA, 4096)
    factors = normal_values(part_keys[3], (NV, ACT, N), (NV * ACT) ** -0.5, 0.09375, ((0, 8), (2, 2)))
    owner = jax.random.permutation(part_keys[4], GROUPS).astype(jnp.int32)
    return {"vectors": vectors, "rotation": rotation, "active": active, "factors": factors, "owner": owner}


def reference(vectors, rotation, active, factors, owner):
    offsets = jnp.arange(B, dtype=jnp.int32)

    def add_vector(total, items):
        vector, blocks, factor = items
        half_rotated = jnp.dot(rotation.T, vector, preferred_element_type=jnp.float32).astype(jnp.bfloat16)
        columns = (blocks[:, None] * B + offsets[None, :]).reshape(-1).astype(jnp.int32)
        picked = jnp.take(rotation, columns, axis=1)
        active_rotated = jnp.dot(half_rotated, picked, preferred_element_type=jnp.float32).astype(jnp.bfloat16)
        return total + jnp.dot(active_rotated, factor, preferred_element_type=jnp.float32), None

    fock, _ = lax.scan(add_vector, jnp.zeros((N, N), jnp.float32), (vectors, active, factors))
    group_rows = N // GROUPS
    return fock.reshape(GROUPS, group_rows, N)[owner].reshape(N, N)
```

```python
import jax
import jax.numpy as jnp
import numpy as np
from jax import lax
from jax.sharding import PartitionSpec as P

B = 128
RING_MAX = 16


def ring_of(mesh):
    devs = mesh.devices
    n = devs.shape[1]
    coords = [getattr(devs[0, v, 0], "coords", None) for v in range(n)]
    if any(c is None for c in coords):
        return list(range(n))
    zs = sorted({c[2] for c in coords})
    xs = sorted({c[0] for c in coords})
    at = {(c[2], c[0]): v for v, c in enumerate(coords)}
    if len(at) != n or len(zs) * len(xs) != n or len(zs) % 2 or len(xs) < 2:
        return list(range(n))
    cycle = [(z, xs[0]) for z in zs]
    for i, z in enumerate(reversed(zs)):
        row = xs[1:] if i % 2 == 0 else xs[1:][::-1]
        cycle += [(z, x) for x in row]
    return [at[c] for c in cycle]


def swap_orb(x, axis):
    other = lax.ppermute(x, "orb", [(0, 1), (1, 0)])
    first = lax.axis_index("orb") == 0
    lo = jnp.where(first, x, other)
    hi = jnp.where(first, other, x)
    return jnp.concatenate([lo, hi], axis=axis)


def ring_all_gather(x, ring):
    n = len(ring)
    right = [(ring[i], ring[(i + 1) % n]) for i in range(n)]
    left = [(ring[i], ring[(i - 1) % n]) for i in range(n)]
    nr = n // 2
    nl = n - 1 - nr
    rb, lb = [], []
    cur = x
    for _ in range(nr):
        cur = lax.ppermute(cur, "vec", right)
        rb.append(cur)
    cur = x
    for _ in range(nl):
        cur = lax.ppermute(cur, "vec", left)
        lb.append(cur)
    stacked = jnp.stack([x] + lb + rb[::-1])
    pos_of = jnp.asarray(np.argsort(np.array(ring)).astype(np.int32))
    pos = pos_of[lax.axis_index("vec")]
    return jnp.take(stacked, (pos_of - pos) % n, axis=0)


def make(mesh):
    ring = ring_of(mesh)
    n = len(ring)
    use_ring = n <= RING_MAX

    def per_device(vectors, rotation, active, factors, owner):
        if use_ring:
            part = ring_all_gather(rotation, ring)
            whole = swap_orb(part, 1).reshape(-1, rotation.shape[1])
        else:
            whole = lax.all_gather(rotation, ("vec", "orb"), axis=0, tiled=True)
        orbitals = whole.shape[0]
        half_rotated = jnp.einsum(
            "sp,gsr->gpr", whole, vectors, preferred_element_type=jnp.float32
        ).astype(jnp.bfloat16)
        full_half = swap_orb(half_rotated, 2)

        columns = (active[:, :, None] * B + jnp.arange(B, dtype=jnp.int32)).reshape(
            active.shape[0], -1
        )
        onehot = (
            jnp.arange(orbitals, dtype=jnp.int32)[None, :, None] == columns[:, None, :]
        ).astype(jnp.bfloat16)
        picked = jnp.einsum(
            "rc,gcj->grj", whole, onehot, preferred_element_type=jnp.float32
        ).astype(jnp.bfloat16)

        active_rotated = jnp.einsum(
            "gpr,grj->gpj", full_half, picked, preferred_element_type=jnp.float32
        ).astype(jnp.bfloat16)

        groups = owner.shape[0]
        group_rows = orbitals // groups
        rows = (owner[:, None] * group_rows + jnp.arange(group_rows, dtype=jnp.int32)).reshape(-1)
        if not use_ring:
            ordered_ar = jnp.take(active_rotated, rows, axis=1)
            ordered = jnp.einsum(
                "gpj,gjq->pq", ordered_ar, factors, preferred_element_type=jnp.float32
            )
            return lax.psum_scatter(ordered, "vec", scatter_dimension=0, tiled=True)

        per = orbitals // n
        blocks = rows.reshape(n, per)
        ring_arr = jnp.asarray(np.array(ring, np.int32))
        pos_of = jnp.asarray(np.argsort(np.array(ring)).astype(np.int32))
        pos = pos_of[lax.axis_index("vec")]
        steps = jnp.arange(n, dtype=jnp.int32)
        rows_r = blocks[ring_arr[(pos - 1 - steps) % n]].reshape(-1)
        rows_l = blocks[ring_arr[(pos + 1 + steps) % n]].reshape(-1)
        cols = factors.shape[2] // 2
        part_r = jnp.einsum(
            "gpj,gjq->pq",
            jnp.take(active_rotated, rows_r, axis=1),
            factors[:, :, :cols],
            preferred_element_type=jnp.float32,
        ).reshape(n, per, cols)
        part_l = jnp.einsum(
            "gpj,gjq->pq",
            jnp.take(active_rotated, rows_l, axis=1),
            factors[:, :, cols:],
            preferred_element_type=jnp.float32,
        ).reshape(n, per, -1)
        right = [(ring[i], ring[(i + 1) % n]) for i in range(n)]
        left = [(ring[i], ring[(i - 1) % n]) for i in range(n)]
        acc_r = part_r[0]
        acc_l = part_l[0]
        for k in range(1, n):
            acc_r = lax.ppermute(acc_r, "vec", right) + part_r[k]
            acc_l = lax.ppermute(acc_l, "vec", left) + part_l[k]
        return jnp.concatenate([acc_r, acc_l], axis=1)

    return per_device


def solution(mesh):
    placed = (
        P(("grp", "vec"), None, "orb"),
        P(("grp", "vec", "orb"), None),
        P(("grp", "vec"), None),
        P(("grp", "vec"), None, "orb"),
        P("grp"),
    )
    return jax.shard_map(
        make(mesh), mesh=mesh, in_specs=placed, out_specs=P(("grp", "vec"), "orb"), check_vma=False
    )
```

```python
import jax
import jax.numpy as jnp
import numpy as np
from jax import lax
from jax.sharding import PartitionSpec as P

B = 128
RING_MAX = 16


def ring_of(mesh):
    devs = mesh.devices
    n = devs.shape[1]
    coords = [getattr(devs[0, v, 0], "coords", None) for v in range(n)]
    if any(c is None for c in coords):
        return list(range(n))
    zs = sorted({c[2] for c in coords})
    xs = sorted({c[0] for c in coords})
    at = {(c[2], c[0]): v for v, c in enumerate(coords)}
    if len(at) != n or len(zs) * len(xs) != n or len(zs) % 2 or len(xs) < 2:
        return list(range(n))
    cycle = [(z, xs[0]) for z in zs]
    for i, z in enumerate(reversed(zs)):
        row = xs[1:] if i % 2 == 0 else xs[1:][::-1]
        cycle += [(z, x) for x in row]
    return [at[c] for c in cycle]


def swap_orb(x, axis):
    other = lax.ppermute(x, "orb", [(0, 1), (1, 0)])
    first = lax.axis_index("orb") == 0
    lo = jnp.where(first, x, other)
    hi = jnp.where(first, other, x)
    return jnp.concatenate([lo, hi], axis=axis)


def ring_all_gather(x, ring):
    n = len(ring)
    right = [(ring[i], ring[(i + 1) % n]) for i in range(n)]
    left = [(ring[i], ring[(i - 1) % n]) for i in range(n)]
    nr = n // 2
    nl = n - 1 - nr
    rb, lb = [], []
    cur = x
    for _ in range(nr):
        cur = lax.ppermute(cur, "vec", right)
        rb.append(cur)
    cur = x
    for _ in range(nl):
        cur = lax.ppermute(cur, "vec", left)
        lb.append(cur)
    stacked = jnp.stack([x] + lb + rb[::-1])
    pos_of = jnp.asarray(np.argsort(np.array(ring)).astype(np.int32))
    pos = pos_of[lax.axis_index("vec")]
    return jnp.take(stacked, (pos_of - pos) % n, axis=0, mode="clip")


def make(mesh):
    ring = ring_of(mesh)
    n = len(ring)
    use_ring = n <= RING_MAX

    def per_device(vectors, rotation, active, factors, owner):
        if use_ring:
            part = ring_all_gather(rotation, ring)
            whole = swap_orb(part, 1).reshape(-1, rotation.shape[1])
        else:
            whole = lax.all_gather(rotation, ("vec", "orb"), axis=0, tiled=True)
        orbitals = whole.shape[0]
        half_rotated = jnp.einsum(
            "sp,gsr->gpr", whole, vectors, preferred_element_type=jnp.float32
        ).astype(jnp.bfloat16)
        other_half = lax.ppermute(half_rotated, "orb", [(0, 1), (1, 0)])

        columns = (active[:, :, None] * B + jnp.arange(B, dtype=jnp.int32)).reshape(
            active.shape[0], -1
        )
        onehot = (
            jnp.arange(orbitals, dtype=jnp.int32)[None, :, None] == columns[:, None, :]
        ).astype(jnp.bfloat16)
        picked = jnp.einsum(
            "rc,gcj->grj", whole, onehot, preferred_element_type=jnp.float32
        ).astype(jnp.bfloat16)
        width = vectors.shape[2]
        first = lax.axis_index("orb") == 0
        lo, hi = picked[:, :width], picked[:, width:]
        mine = jnp.where(first, lo, hi)
        theirs = jnp.where(first, hi, lo)
        active_rotated = (
            jnp.einsum("gpr,grj->gpj", half_rotated, mine, preferred_element_type=jnp.float32)
            + jnp.einsum("gpr,grj->gpj", other_half, theirs, preferred_element_type=jnp.float32)
        ).astype(jnp.bfloat16)

        groups = owner.shape[0]
        group_rows = orbitals // groups
        rows = (owner[:, None] * group_rows + jnp.arange(group_rows, dtype=jnp.int32)).reshape(-1)
        if not use_ring:
            ordered_ar = jnp.take(active_rotated, rows, axis=1)
            ordered = jnp.einsum(
                "gpj,gjq->pq", ordered_ar, factors, preferred_element_type=jnp.float32
            )
            return lax.psum_scatter(ordered, "vec", scatter_dimension=0, tiled=True)

        per = orbitals // n
        held = owner.reshape(n, -1)
        ring_arr = jnp.asarray(np.array(ring, np.int32))
        pos_of = jnp.asarray(np.argsort(np.array(ring)).astype(np.int32))
        pos = pos_of[lax.axis_index("vec")]
        steps = jnp.arange(n, dtype=jnp.int32)
        by_group = active_rotated.reshape(active_rotated.shape[0], groups, group_rows, -1)

        def in_step_order(order):
            picked_groups = held[ring_arr[order % n]].reshape(-1)
            taken = jnp.take(by_group, picked_groups, axis=1, mode="clip")
            return taken.reshape(active_rotated.shape)

        cols = factors.shape[2] // 2
        part_r = jnp.einsum(
            "gpj,gjq->pq",
            in_step_order(pos - 1 - steps),
            factors[:, :, :cols],
            preferred_element_type=jnp.float32,
        ).reshape(n, per, cols)
        part_l = jnp.einsum(
            "gpj,gjq->pq",
            in_step_order(pos + 1 + steps),
            factors[:, :, cols:],
            preferred_element_type=jnp.float32,
        ).reshape(n, per, -1)
        right = [(ring[i], ring[(i + 1) % n]) for i in range(n)]
        left = [(ring[i], ring[(i - 1) % n]) for i in range(n)]
        acc_r = part_r[0]
        acc_l = part_l[0]
        for k in range(1, n):
            acc_r = lax.ppermute(acc_r, "vec", right) + part_r[k]
            acc_l = lax.ppermute(acc_l, "vec", left) + part_l[k]
        return jnp.concatenate([acc_r, acc_l], axis=1)

    return per_device


def solution(mesh):
    placed = (
        P(("grp", "vec"), None, "orb"),
        P(("grp", "vec", "orb"), None),
        P(("grp", "vec"), None),
        P(("grp", "vec"), None, "orb"),
        P("grp"),
    )
    return jax.shard_map(
        make(mesh), mesh=mesh, in_specs=placed, out_specs=P(("grp", "vec"), "orb"), check_vma=False
    )
```

```python
import jax
import jax.numpy as jnp
import numpy as np
from jax import lax
from jax.sharding import PartitionSpec as P

B = 128
RING_MAX = 16


def ring_of(mesh):
    devs = mesh.devices
    n = devs.shape[1]
    coords = [getattr(devs[0, v, 0], "coords", None) for v in range(n)]
    if any(c is None for c in coords):
        return list(range(n))
    zs = sorted({c[2] for c in coords})
    xs = sorted({c[0] for c in coords})
    at = {(c[2], c[0]): v for v, c in enumerate(coords)}
    if len(at) != n or len(zs) * len(xs) != n or len(zs) % 2 or len(xs) < 2:
        return list(range(n))
    cycle = [(z, xs[0]) for z in zs]
    for i, z in enumerate(reversed(zs)):
        row = xs[1:] if i % 2 == 0 else xs[1:][::-1]
        cycle += [(z, x) for x in row]
    return [at[c] for c in cycle]


def swap_orb(x, axis):
    other = lax.ppermute(x, "orb", [(0, 1), (1, 0)])
    first = lax.axis_index("orb") == 0
    lo = jnp.where(first, x, other)
    hi = jnp.where(first, other, x)
    return jnp.concatenate([lo, hi], axis=axis)


def ring_all_gather(x, ring):
    n = len(ring)
    right = [(ring[i], ring[(i + 1) % n]) for i in range(n)]
    left = [(ring[i], ring[(i - 1) % n]) for i in range(n)]
    nr = n // 2
    nl = n - 1 - nr
    rb, lb = [], []
    cur = x
    for _ in range(nr):
        cur = lax.ppermute(cur, "vec", right)
        rb.append(cur)
    cur = x
    for _ in range(nl):
        cur = lax.ppermute(cur, "vec", left)
        lb.append(cur)
    stacked = jnp.stack([x] + lb + rb[::-1])
    pos_of = jnp.asarray(np.argsort(np.array(ring)).astype(np.int32))
    pos = pos_of[lax.axis_index("vec")]
    return jnp.take(stacked, (pos_of - pos) % n, axis=0, mode="clip")


def make(mesh):
    ring = ring_of(mesh)
    n = len(ring)
    use_ring = n <= RING_MAX

    def per_device(vectors, rotation, active, factors, owner):
        if use_ring:
            part = ring_all_gather(rotation, ring)
            whole = swap_orb(part, 1).reshape(-1, rotation.shape[1])
        else:
            whole = lax.all_gather(rotation, ("vec", "orb"), axis=0, tiled=True)
        orbitals = whole.shape[0]
        half_rotated = jnp.einsum(
            "sp,gsr->gpr", whole, vectors, preferred_element_type=jnp.float32
        ).astype(jnp.bfloat16)
        other_half = lax.ppermute(half_rotated, "orb", [(0, 1), (1, 0)])

        columns = (active[:, :, None] * B + jnp.arange(B, dtype=jnp.int32)).reshape(
            active.shape[0], -1
        )
        onehot = (
            jnp.arange(orbitals, dtype=jnp.int32)[None, :, None] == columns[:, None, :]
        ).astype(jnp.bfloat16)
        picked = jnp.einsum(
            "rc,gcj->grj", whole, onehot, preferred_element_type=jnp.float32
        ).astype(jnp.bfloat16)
        width = vectors.shape[2]
        first = lax.axis_index("orb") == 0
        lo, hi = picked[:, :width], picked[:, width:]
        mine = jnp.where(first, lo, hi)
        theirs = jnp.where(first, hi, lo)
        active_rotated = (
            jnp.einsum("gpr,grj->gpj", half_rotated, mine, preferred_element_type=jnp.float32)
            + jnp.einsum("gpr,grj->gpj", other_half, theirs, preferred_element_type=jnp.float32)
        ).astype(jnp.bfloat16)

        groups = owner.shape[0]
        group_rows = orbitals // groups
        rows = (owner[:, None] * group_rows + jnp.arange(group_rows, dtype=jnp.int32)).reshape(-1)
        if not use_ring:
            ordered_ar = jnp.take(active_rotated, rows, axis=1)
            ordered = jnp.einsum(
                "gpj,gjq->pq", ordered_ar, factors, preferred_element_type=jnp.float32
            )
            return lax.psum_scatter(ordered, "vec", scatter_dimension=0, tiled=True)

        per = orbitals // n
        held = owner.reshape(n, -1)
        ring_arr = jnp.asarray(np.array(ring, np.int32))
        pos_of = jnp.asarray(np.argsort(np.array(ring)).astype(np.int32))
        pos = pos_of[lax.axis_index("vec")]
        steps = jnp.arange(n, dtype=jnp.int32)
        by_group = active_rotated.reshape(active_rotated.shape[0], groups, group_rows, -1)

        def in_step_order(order):
            picked_groups = held[ring_arr[order % n]].reshape(-1)
            taken = jnp.take(by_group, picked_groups, axis=1, mode="clip")
            return taken.reshape(active_rotated.shape)

        ordered = in_step_order(pos - 1 - steps)
        cols = factors.shape[2] // 2
        part_r = jnp.einsum(
            "gpj,gjq->pq", ordered, factors[:, :, :cols], preferred_element_type=jnp.float32
        ).reshape(n, per, cols)
        part_l = jnp.einsum(
            "gpj,gjq->pq", ordered, factors[:, :, cols:], preferred_element_type=jnp.float32
        ).reshape(n, per, -1)
        right = [(ring[i], ring[(i + 1) % n]) for i in range(n)]
        left = [(ring[i], ring[(i - 1) % n]) for i in range(n)]
        acc_r = part_r[0]
        acc_l = part_l[n - 2]
        for k in range(1, n):
            acc_r = lax.ppermute(acc_r, "vec", right) + part_r[k]
            acc_l = lax.ppermute(acc_l, "vec", left) + part_l[n - 2 - k if k < n - 1 else n - 1]
        return jnp.concatenate([acc_r, acc_l], axis=1)

    return per_device


def solution(mesh):
    placed = (
        P(("grp", "vec"), None, "orb"),
        P(("grp", "vec", "orb"), None),
        P(("grp", "vec"), None),
        P(("grp", "vec"), None, "orb"),
        P("grp"),
    )
    return jax.shard_map(
        make(mesh), mesh=mesh, in_specs=placed, out_specs=P(("grp", "vec"), "orb"), check_vma=False
    )
```

```python
import jax
import jax.numpy as jnp
import numpy as np
from jax import lax
from jax.sharding import PartitionSpec as P

B = 128
RING_MAX = 16


def ring_of(mesh):
    devs = mesh.devices
    n = devs.shape[1]
    coords = [getattr(devs[0, v, 0], "coords", None) for v in range(n)]
    if any(c is None for c in coords):
        return list(range(n))
    zs = sorted({c[2] for c in coords})
    xs = sorted({c[0] for c in coords})
    at = {(c[2], c[0]): v for v, c in enumerate(coords)}
    if len(at) != n or len(zs) * len(xs) != n or len(zs) % 2 or len(xs) < 2:
        return list(range(n))
    cycle = [(z, xs[0]) for z in zs]
    for i, z in enumerate(reversed(zs)):
        row = xs[1:] if i % 2 == 0 else xs[1:][::-1]
        cycle += [(z, x) for x in row]
    return [at[c] for c in cycle]


def swap_orb(x, axis):
    other = lax.ppermute(x, "orb", [(0, 1), (1, 0)])
    first = lax.axis_index("orb") == 0
    lo = jnp.where(first, x, other)
    hi = jnp.where(first, other, x)
    return jnp.concatenate([lo, hi], axis=axis)


def ring_all_gather(x, ring):
    n = len(ring)
    right = [(ring[i], ring[(i + 1) % n]) for i in range(n)]
    left = [(ring[i], ring[(i - 1) % n]) for i in range(n)]
    nr = n // 2
    nl = n - 1 - nr
    rb, lb = [], []
    cur = x
    for _ in range(nr):
        cur = lax.ppermute(cur, "vec", right)
        rb.append(cur)
    cur = x
    for _ in range(nl):
        cur = lax.ppermute(cur, "vec", left)
        lb.append(cur)
    got = [x] + lb + rb[::-1]
    pos_of = jnp.asarray(np.argsort(np.array(ring)).astype(np.int32))
    pos = pos_of[lax.axis_index("vec")]
    offset = ((pos_of - pos) % n)[:, None, None]
    out = jnp.zeros((n,) + x.shape, x.dtype)
    for d, block in enumerate(got):
        out = jnp.where(offset == d, block[None], out)
    return out


def make(mesh):
    ring = ring_of(mesh)
    n = len(ring)
    use_ring = n <= RING_MAX

    def per_device(vectors, rotation, active, factors, owner):
        if use_ring:
            part = ring_all_gather(rotation, ring)
            whole = swap_orb(part, 1).reshape(-1, rotation.shape[1])
        else:
            whole = lax.all_gather(rotation, ("vec", "orb"), axis=0, tiled=True)
        orbitals = whole.shape[0]
        half_rotated = jnp.einsum(
            "sp,gsr->gpr", whole, vectors, preferred_element_type=jnp.float32
        ).astype(jnp.bfloat16)
        other_half = lax.ppermute(half_rotated, "orb", [(0, 1), (1, 0)])

        columns = (active[:, :, None] * B + jnp.arange(B, dtype=jnp.int32)).reshape(
            active.shape[0], -1
        )
        onehot = (
            jnp.arange(orbitals, dtype=jnp.int32)[None, :, None] == columns[:, None, :]
        ).astype(jnp.bfloat16)
        picked = jnp.einsum(
            "rc,gcj->grj", whole, onehot, preferred_element_type=jnp.float32
        ).astype(jnp.bfloat16)
        width = vectors.shape[2]
        first = lax.axis_index("orb") == 0
        lo, hi = picked[:, :width], picked[:, width:]
        mine = jnp.where(first, lo, hi)
        theirs = jnp.where(first, hi, lo)
        active_rotated = (
            jnp.einsum("gpr,grj->gpj", half_rotated, mine, preferred_element_type=jnp.float32)
            + jnp.einsum("gpr,grj->gpj", other_half, theirs, preferred_element_type=jnp.float32)
        ).astype(jnp.bfloat16)

        groups = owner.shape[0]
        group_rows = orbitals // groups
        rows = (owner[:, None] * group_rows + jnp.arange(group_rows, dtype=jnp.int32)).reshape(-1)
        if not use_ring:
            ordered_ar = jnp.take(active_rotated, rows, axis=1)
            ordered = jnp.einsum(
                "gpj,gjq->pq", ordered_ar, factors, preferred_element_type=jnp.float32
            )
            return lax.psum_scatter(ordered, "vec", scatter_dimension=0, tiled=True)

        per = orbitals // n
        held = owner.reshape(n, -1)
        ring_arr = jnp.asarray(np.array(ring, np.int32))
        pos_of = jnp.asarray(np.argsort(np.array(ring)).astype(np.int32))
        pos = pos_of[lax.axis_index("vec")]
        steps = jnp.arange(n, dtype=jnp.int32)
        by_group = active_rotated.reshape(active_rotated.shape[0], groups, group_rows, -1)

        def in_step_order(order):
            picked_groups = held[ring_arr[order % n]].reshape(-1)
            taken = jnp.take(by_group, picked_groups, axis=1, mode="clip")
            return taken.reshape(active_rotated.shape)

        ordered = in_step_order(pos - 1 - steps)
        cols = factors.shape[2] // 2
        part_r = jnp.einsum(
            "gpj,gjq->pq", ordered, factors[:, :, :cols], preferred_element_type=jnp.float32
        ).reshape(n, per, cols)
        part_l = jnp.einsum(
            "gpj,gjq->pq", ordered, factors[:, :, cols:], preferred_element_type=jnp.float32
        ).reshape(n, per, -1)
        right = [(ring[i], ring[(i + 1) % n]) for i in range(n)]
        left = [(ring[i], ring[(i - 1) % n]) for i in range(n)]
        acc_r = part_r[0]
        acc_l = part_l[n - 2]
        for k in range(1, n):
            acc_r = lax.ppermute(acc_r, "vec", right) + part_r[k]
            acc_l = lax.ppermute(acc_l, "vec", left) + part_l[n - 2 - k if k < n - 1 else n - 1]
        return jnp.concatenate([acc_r, acc_l], axis=1)

    return per_device


def solution(mesh):
    placed = (
        P(("grp", "vec"), None, "orb"),
        P(("grp", "vec", "orb"), None),
        P(("grp", "vec"), None),
        P(("grp", "vec"), None, "orb"),
        P("grp"),
    )
    return jax.shard_map(
        make(mesh), mesh=mesh, in_specs=placed, out_specs=P(("grp", "vec"), "orb"), check_vma=False
    )
```

```python
import jax
import jax.numpy as jnp
import numpy as np
from jax import lax
from jax.sharding import PartitionSpec as P

B = 128
RING_MAX = 16


def ring_of(mesh):
    devs = mesh.devices
    n = devs.shape[1]
    coords = [getattr(devs[0, v, 0], "coords", None) for v in range(n)]
    if any(c is None for c in coords):
        return list(range(n))
    zs = sorted({c[2] for c in coords})
    xs = sorted({c[0] for c in coords})
    at = {(c[2], c[0]): v for v, c in enumerate(coords)}
    if len(at) != n or len(zs) * len(xs) != n or len(zs) % 2 or len(xs) < 2:
        return list(range(n))
    cycle = [(z, xs[0]) for z in zs]
    for i, z in enumerate(reversed(zs)):
        row = xs[1:] if i % 2 == 0 else xs[1:][::-1]
        cycle += [(z, x) for x in row]
    return [at[c] for c in cycle]


def swap_orb(x, axis):
    other = lax.ppermute(x, "orb", [(0, 1), (1, 0)])
    first = lax.axis_index("orb") == 0
    lo = jnp.where(first, x, other)
    hi = jnp.where(first, other, x)
    return jnp.concatenate([lo, hi], axis=axis)


def ring_all_gather(x, ring):
    n = len(ring)
    right = [(ring[i], ring[(i + 1) % n]) for i in range(n)]
    left = [(ring[i], ring[(i - 1) % n]) for i in range(n)]
    nr = n // 2
    nl = n - 1 - nr
    rb, lb = [], []
    cur = x
    for _ in range(nr):
        cur = lax.ppermute(cur, "vec", right)
        rb.append(cur)
    cur = x
    for _ in range(nl):
        cur = lax.ppermute(cur, "vec", left)
        lb.append(cur)
    got = [x] + lb + rb[::-1]
    theirs = lax.ppermute(tuple(got), "orb", [(0, 1), (1, 0)])
    pos_of = jnp.asarray(np.argsort(np.array(ring)).astype(np.int32))
    pos = pos_of[lax.axis_index("vec")]
    offset = ((pos_of - pos) % n)[:, None, None, None]
    first = lax.axis_index("orb") == 0
    out = jnp.zeros((n, 2) + x.shape, x.dtype)
    for d in range(n):
        pair = jnp.where(first, jnp.stack([got[d], theirs[d]]), jnp.stack([theirs[d], got[d]]))
        out = jnp.where(offset == d, pair[None], out)
    return out


def make(mesh):
    ring = ring_of(mesh)
    n = len(ring)
    use_ring = n <= RING_MAX

    def per_device(vectors, rotation, active, factors, owner):
        if use_ring:
            whole = ring_all_gather(rotation, ring).reshape(-1, rotation.shape[1])
        else:
            whole = lax.all_gather(rotation, ("vec", "orb"), axis=0, tiled=True)
        orbitals = whole.shape[0]
        half_rotated = jnp.einsum(
            "sp,gsr->gpr", whole, vectors, preferred_element_type=jnp.float32
        ).astype(jnp.bfloat16)
        other_half = lax.ppermute(half_rotated, "orb", [(0, 1), (1, 0)])

        columns = (active[:, :, None] * B + jnp.arange(B, dtype=jnp.int32)).reshape(
            active.shape[0], -1
        )
        onehot = (
            jnp.arange(orbitals, dtype=jnp.int32)[None, :, None] == columns[:, None, :]
        ).astype(jnp.bfloat16)
        picked = jnp.einsum(
            "rc,gcj->grj", whole, onehot, preferred_element_type=jnp.float32
        ).astype(jnp.bfloat16)
        width = vectors.shape[2]
        first = lax.axis_index("orb") == 0
        lo, hi = picked[:, :width], picked[:, width:]
        mine = jnp.where(first, lo, hi)
        theirs = jnp.where(first, hi, lo)
        active_rotated = (
            jnp.einsum("gpr,grj->gpj", half_rotated, mine, preferred_element_type=jnp.float32)
            + jnp.einsum("gpr,grj->gpj", other_half, theirs, preferred_element_type=jnp.float32)
        ).astype(jnp.bfloat16)

        groups = owner.shape[0]
        group_rows = orbitals // groups
        rows = (owner[:, None] * group_rows + jnp.arange(group_rows, dtype=jnp.int32)).reshape(-1)
        if not use_ring:
            ordered_ar = jnp.take(active_rotated, rows, axis=1)
            ordered = jnp.einsum(
                "gpj,gjq->pq", ordered_ar, factors, preferred_element_type=jnp.float32
            )
            return lax.psum_scatter(ordered, "vec", scatter_dimension=0, tiled=True)

        per = orbitals // n
        held = owner.reshape(n, -1)
        ring_arr = jnp.asarray(np.array(ring, np.int32))
        pos_of = jnp.asarray(np.argsort(np.array(ring)).astype(np.int32))
        pos = pos_of[lax.axis_index("vec")]
        steps = jnp.arange(n, dtype=jnp.int32)
        by_group = active_rotated.reshape(active_rotated.shape[0], groups, group_rows, -1)

        def in_step_order(order):
            picked_groups = held[ring_arr[order % n]].reshape(-1)
            taken = jnp.take(by_group, picked_groups, axis=1, mode="clip")
            return taken.reshape(active_rotated.shape)

        ordered = in_step_order(pos - 1 - steps)
        cols = factors.shape[2] // 2
        part_r = jnp.einsum(
            "gpj,gjq->pq", ordered, factors[:, :, :cols], preferred_element_type=jnp.float32
        ).reshape(n, per, cols)
        part_l = jnp.einsum(
            "gpj,gjq->pq", ordered, factors[:, :, cols:], preferred_element_type=jnp.float32
        ).reshape(n, per, -1)
        right = [(ring[i], ring[(i + 1) % n]) for i in range(n)]
        left = [(ring[i], ring[(i - 1) % n]) for i in range(n)]
        acc_r = part_r[0]
        acc_l = part_l[n - 2]
        for k in range(1, n):
            acc_r = lax.ppermute(acc_r, "vec", right) + part_r[k]
            acc_l = lax.ppermute(acc_l, "vec", left) + part_l[n - 2 - k if k < n - 1 else n - 1]
        return jnp.concatenate([acc_r, acc_l], axis=1)

    return per_device


def solution(mesh):
    placed = (
        P(("grp", "vec"), None, "orb"),
        P(("grp", "vec", "orb"), None),
        P(("grp", "vec"), None),
        P(("grp", "vec"), None, "orb"),
        P("grp"),
    )
    return jax.shard_map(
        make(mesh), mesh=mesh, in_specs=placed, out_specs=P(("grp", "vec"), "orb"), check_vma=False
    )
```

```python
import jax
import jax.numpy as jnp
import numpy as np
from jax import lax
from jax.sharding import PartitionSpec as P

B = 128
RING_MAX = 16


def ring_of(mesh):
    devs = mesh.devices
    n = devs.shape[1]
    coords = [getattr(devs[0, v, 0], "coords", None) for v in range(n)]
    if any(c is None for c in coords):
        return list(range(n))
    zs = sorted({c[2] for c in coords})
    xs = sorted({c[0] for c in coords})
    at = {(c[2], c[0]): v for v, c in enumerate(coords)}
    if len(at) != n or len(zs) * len(xs) != n or len(zs) % 2 or len(xs) < 2:
        return list(range(n))
    cycle = [(z, xs[0]) for z in zs]
    for i, z in enumerate(reversed(zs)):
        row = xs[1:] if i % 2 == 0 else xs[1:][::-1]
        cycle += [(z, x) for x in row]
    return [at[c] for c in cycle]


def swap_orb(x, axis):
    other = lax.ppermute(x, "orb", [(0, 1), (1, 0)])
    first = lax.axis_index("orb") == 0
    lo = jnp.where(first, x, other)
    hi = jnp.where(first, other, x)
    return jnp.concatenate([lo, hi], axis=axis)


def ring_all_gather(x, ring):
    n = len(ring)
    right = [(ring[i], ring[(i + 1) % n]) for i in range(n)]
    left = [(ring[i], ring[(i - 1) % n]) for i in range(n)]
    nr = n // 2
    nl = n - 1 - nr
    rb, lb = [], []
    cur = x
    for _ in range(nr):
        cur = lax.ppermute(cur, "vec", right)
        rb.append(cur)
    cur = x
    for _ in range(nl):
        cur = lax.ppermute(cur, "vec", left)
        lb.append(cur)
    got = [x] + lb + rb[::-1]
    theirs = lax.ppermute(tuple(got), "orb", [(0, 1), (1, 0)])
    pos_of = jnp.asarray(np.argsort(np.array(ring)).astype(np.int32))
    pos = pos_of[lax.axis_index("vec")]
    offset = ((pos_of - pos) % n)[:, None, None, None]
    first = lax.axis_index("orb") == 0
    out = jnp.zeros((n, 2) + x.shape, x.dtype)
    for d in range(n):
        pair = jnp.where(first, jnp.stack([got[d], theirs[d]]), jnp.stack([theirs[d], got[d]]))
        out = jnp.where(offset == d, pair[None], out)
    return out


def make(mesh):
    ring = ring_of(mesh)
    n = len(ring)
    use_ring = n <= RING_MAX

    def per_device(vectors, rotation, active, factors, owner):
        if use_ring:
            whole = ring_all_gather(rotation, ring).reshape(-1, rotation.shape[1])
        else:
            whole = lax.all_gather(rotation, ("vec", "orb"), axis=0, tiled=True)
        orbitals = whole.shape[0]
        half_rotated = jnp.einsum(
            "sp,gsr->gpr", whole, vectors, preferred_element_type=jnp.float32
        ).astype(jnp.bfloat16)
        other_half = lax.ppermute(half_rotated, "orb", [(0, 1), (1, 0)])

        columns = (active[:, :, None] * B + jnp.arange(B, dtype=jnp.int32)).reshape(
            active.shape[0], -1
        )
        onehot = (
            jnp.arange(orbitals, dtype=jnp.int32)[None, :, None] == columns[:, None, :]
        ).astype(jnp.bfloat16)
        picked = jnp.einsum(
            "rc,gcj->grj", whole, onehot, preferred_element_type=jnp.float32
        ).astype(jnp.bfloat16)
        width = vectors.shape[2]
        first = lax.axis_index("orb") == 0
        lo, hi = picked[:, :width], picked[:, width:]
        mine = jnp.where(first, lo, hi)
        theirs = jnp.where(first, hi, lo)
        active_rotated = (
            jnp.einsum("gpr,grj->gpj", half_rotated, mine, preferred_element_type=jnp.float32)
            + jnp.einsum("gpr,grj->gpj", other_half, theirs, preferred_element_type=jnp.float32)
        ).astype(jnp.bfloat16)

        groups = owner.shape[0]
        group_rows = orbitals // groups
        rows = (owner[:, None] * group_rows + jnp.arange(group_rows, dtype=jnp.int32)).reshape(-1)
        if not use_ring:
            ordered_ar = jnp.take(active_rotated, rows, axis=1)
            ordered = jnp.einsum(
                "gpj,gjq->pq", ordered_ar, factors, preferred_element_type=jnp.float32
            )
            return lax.psum_scatter(ordered, "vec", scatter_dimension=0, tiled=True)

        per = orbitals // n
        held = owner.reshape(n, -1)
        by_group = active_rotated.reshape(active_rotated.shape[0], groups, group_rows, -1)
        me = lax.axis_index("vec")
        table = np.array([[ring[(p - 1 - k) % n] for k in range(n)] for p in range(n)], np.int32)
        pos_of = np.argsort(np.array(ring))
        by_vec = jnp.asarray(table[pos_of])
        hits = (jnp.arange(n, dtype=jnp.int32) == me)[:, None]
        dest = jnp.sum(jnp.where(hits, by_vec, 0), axis=0)
        order = jnp.sum(
            jnp.where(dest[:, None, None] == jnp.arange(n, dtype=jnp.int32)[None, :, None], held[None], 0),
            axis=1,
        ).reshape(-1)
        ordered = jnp.take(by_group, order, axis=1, mode="clip").reshape(active_rotated.shape)
        cols = factors.shape[2] // 2
        part_r = jnp.einsum(
            "gpj,gjq->pq", ordered, factors[:, :, :cols], preferred_element_type=jnp.float32
        ).reshape(n, per, cols)
        part_l = jnp.einsum(
            "gpj,gjq->pq", ordered, factors[:, :, cols:], preferred_element_type=jnp.float32
        ).reshape(n, per, -1)
        right = [(ring[i], ring[(i + 1) % n]) for i in range(n)]
        left = [(ring[i], ring[(i - 1) % n]) for i in range(n)]
        acc_r = part_r[0]
        acc_l = part_l[n - 2]
        for k in range(1, n):
            acc_r = lax.ppermute(acc_r, "vec", right) + part_r[k]
            acc_l = lax.ppermute(acc_l, "vec", left) + part_l[n - 2 - k if k < n - 1 else n - 1]
        return jnp.concatenate([acc_r, acc_l], axis=1)

    return per_device


def solution(mesh):
    placed = (
        P(("grp", "vec"), None, "orb"),
        P(("grp", "vec", "orb"), None),
        P(("grp", "vec"), None),
        P(("grp", "vec"), None, "orb"),
        P("grp"),
    )
    return jax.shard_map(
        make(mesh), mesh=mesh, in_specs=placed, out_specs=P(("grp", "vec"), "orb"), check_vma=False
    )
```

```python
import jax
import jax.numpy as jnp
import numpy as np
from jax import lax
from jax.sharding import PartitionSpec as P

B = 128
RING_MAX = 16


def ring_of(mesh):
    devs = mesh.devices
    n = devs.shape[1]
    coords = [getattr(devs[0, v, 0], "coords", None) for v in range(n)]
    if any(c is None for c in coords):
        return list(range(n))
    zs = sorted({c[2] for c in coords})
    xs = sorted({c[0] for c in coords})
    at = {(c[2], c[0]): v for v, c in enumerate(coords)}
    if len(at) != n or len(zs) * len(xs) != n or len(zs) % 2 or len(xs) < 2:
        return list(range(n))
    cycle = [(z, xs[0]) for z in zs]
    for i, z in enumerate(reversed(zs)):
        row = xs[1:] if i % 2 == 0 else xs[1:][::-1]
        cycle += [(z, x) for x in row]
    return [at[c] for c in cycle]


def swap_orb(x, axis):
    other = lax.ppermute(x, "orb", [(0, 1), (1, 0)])
    first = lax.axis_index("orb") == 0
    lo = jnp.where(first, x, other)
    hi = jnp.where(first, other, x)
    return jnp.concatenate([lo, hi], axis=axis)


def ring_all_gather(x, ring):
    n = len(ring)
    right = [(ring[i], ring[(i + 1) % n]) for i in range(n)]
    left = [(ring[i], ring[(i - 1) % n]) for i in range(n)]
    nr = n // 2
    nl = n - 1 - nr
    rb, lb = [], []
    cur = x
    for _ in range(nr):
        cur = lax.ppermute(cur, "vec", right)
        rb.append(cur)
    cur = x
    for _ in range(nl):
        cur = lax.ppermute(cur, "vec", left)
        lb.append(cur)
    got = [x] + lb + rb[::-1]
    theirs = lax.ppermute(tuple(got), "orb", [(0, 1), (1, 0)])
    pos_of = jnp.asarray(np.argsort(np.array(ring)).astype(np.int32))
    pos = pos_of[lax.axis_index("vec")]
    offset = ((pos_of - pos) % n)[:, None, None, None]
    first = lax.axis_index("orb") == 0
    out = jnp.zeros((n, 2) + x.shape, x.dtype)
    for d in range(n):
        pair = jnp.where(first, jnp.stack([got[d], theirs[d]]), jnp.stack([theirs[d], got[d]]))
        out = jnp.where(offset == d, pair[None], out)
    return out


def make(mesh):
    ring = ring_of(mesh)
    n = len(ring)
    use_ring = n <= RING_MAX

    def per_device(vectors, rotation, active, factors, owner):
        if use_ring:
            whole = ring_all_gather(rotation, ring).reshape(-1, rotation.shape[1])
        else:
            whole = lax.all_gather(rotation, ("vec", "orb"), axis=0, tiled=True)
        orbitals = whole.shape[0]
        halves = [
            jnp.einsum("sp,sr->pr", whole, v, preferred_element_type=jnp.float32).astype(jnp.bfloat16)
            for v in vectors
        ]
        other_half = jnp.stack([lax.ppermute(h, "orb", [(0, 1), (1, 0)]) for h in halves])
        half_rotated = jnp.stack(halves)

        columns = (active[:, :, None] * B + jnp.arange(B, dtype=jnp.int32)).reshape(
            active.shape[0], -1
        )
        onehot = (
            jnp.arange(orbitals, dtype=jnp.int32)[None, :, None] == columns[:, None, :]
        ).astype(jnp.bfloat16)
        picked = jnp.einsum(
            "rc,gcj->grj", whole, onehot, preferred_element_type=jnp.float32
        ).astype(jnp.bfloat16)
        width = vectors.shape[2]
        first = lax.axis_index("orb") == 0
        lo, hi = picked[:, :width], picked[:, width:]
        mine = jnp.where(first, lo, hi)
        theirs = jnp.where(first, hi, lo)
        active_rotated = (
            jnp.einsum("gpr,grj->gpj", half_rotated, mine, preferred_element_type=jnp.float32)
            + jnp.einsum("gpr,grj->gpj", other_half, theirs, preferred_element_type=jnp.float32)
        ).astype(jnp.bfloat16)

        groups = owner.shape[0]
        group_rows = orbitals // groups
        rows = (owner[:, None] * group_rows + jnp.arange(group_rows, dtype=jnp.int32)).reshape(-1)
        if not use_ring:
            ordered_ar = jnp.take(active_rotated, rows, axis=1)
            ordered = jnp.einsum(
                "gpj,gjq->pq", ordered_ar, factors, preferred_element_type=jnp.float32
            )
            return lax.psum_scatter(ordered, "vec", scatter_dimension=0, tiled=True)

        per = orbitals // n
        held = owner.reshape(n, -1)
        by_group = active_rotated.reshape(active_rotated.shape[0], groups, group_rows, -1)
        me = lax.axis_index("vec")
        reach = n // 2
        back = n - 1 - reach
        shifts = list(range(reach, 0, -1)) + list(range(-back, 0)) + [0]
        table = np.array([[ring[(p + d) % n] for d in shifts] for p in range(n)], np.int32)
        pos_of = np.argsort(np.array(ring))
        by_vec = jnp.asarray(table[pos_of])
        hits = (jnp.arange(n, dtype=jnp.int32) == me)[:, None]
        dest = jnp.sum(jnp.where(hits, by_vec, 0), axis=0)
        order = jnp.sum(
            jnp.where(dest[:, None, None] == jnp.arange(n, dtype=jnp.int32)[None, :, None], held[None], 0),
            axis=1,
        ).reshape(-1)
        ordered = jnp.take(by_group, order, axis=1, mode="clip").reshape(active_rotated.shape)
        part = jnp.einsum(
            "gpj,gjq->pq", ordered, factors, preferred_element_type=jnp.float32
        ).reshape(n, per, -1)
        right = [(ring[i], ring[(i + 1) % n]) for i in range(n)]
        left = [(ring[i], ring[(i - 1) % n]) for i in range(n)]
        total = part[n - 1]
        acc = part[0]
        for k in range(1, reach):
            acc = lax.ppermute(acc, "vec", right) + part[k]
        total = total + lax.ppermute(acc, "vec", right)
        if back:
            acc = part[reach]
            for k in range(1, back):
                acc = lax.ppermute(acc, "vec", left) + part[reach + k]
            total = total + lax.ppermute(acc, "vec", left)
        return total

    return per_device


def solution(mesh):
    placed = (
        P(("grp", "vec"), None, "orb"),
        P(("grp", "vec", "orb"), None),
        P(("grp", "vec"), None),
        P(("grp", "vec"), None, "orb"),
        P("grp"),
    )
    return jax.shard_map(
        make(mesh), mesh=mesh, in_specs=placed, out_specs=P(("grp", "vec"), "orb"), check_vma=False
    )
```

```python
import jax
import jax.numpy as jnp
import numpy as np
from jax import lax
from jax.sharding import PartitionSpec as P

B = 128
RING_MAX = 16


def ring_of(mesh):
    devs = mesh.devices
    n = devs.shape[1]
    coords = [getattr(devs[0, v, 0], "coords", None) for v in range(n)]
    if any(c is None for c in coords):
        return list(range(n))
    zs = sorted({c[2] for c in coords})
    xs = sorted({c[0] for c in coords})
    at = {(c[2], c[0]): v for v, c in enumerate(coords)}
    if len(at) != n or len(zs) * len(xs) != n or len(zs) % 2 or len(xs) < 2:
        return list(range(n))
    cycle = [(z, xs[0]) for z in zs]
    for i, z in enumerate(reversed(zs)):
        row = xs[1:] if i % 2 == 0 else xs[1:][::-1]
        cycle += [(z, x) for x in row]
    return [at[c] for c in cycle]


def swap_orb(x, axis):
    other = lax.ppermute(x, "orb", [(0, 1), (1, 0)])
    first = lax.axis_index("orb") == 0
    lo = jnp.where(first, x, other)
    hi = jnp.where(first, other, x)
    return jnp.concatenate([lo, hi], axis=axis)


def ring_all_gather(x, ring):
    n = len(ring)
    right = [(ring[i], ring[(i + 1) % n]) for i in range(n)]
    left = [(ring[i], ring[(i - 1) % n]) for i in range(n)]
    nr = n // 2
    nl = n - 1 - nr
    rb, lb = [], []
    cur = x
    for _ in range(nr):
        cur = lax.ppermute(cur, "vec", right)
        rb.append(cur)
    cur = x
    for _ in range(nl):
        cur = lax.ppermute(cur, "vec", left)
        lb.append(cur)
    got = [x] + lb + rb[::-1]
    theirs = lax.ppermute(tuple(got), "orb", [(0, 1), (1, 0)])
    pos_of = jnp.asarray(np.argsort(np.array(ring)).astype(np.int32))
    pos = pos_of[lax.axis_index("vec")]
    offset = ((pos_of - pos) % n)[:, None, None, None]
    first = lax.axis_index("orb") == 0
    out = jnp.zeros((n, 2) + x.shape, x.dtype)
    for d in range(n):
        pair = jnp.where(first, jnp.stack([got[d], theirs[d]]), jnp.stack([theirs[d], got[d]]))
        out = jnp.where(offset == d, pair[None], out)
    return out


def make(mesh):
    ring = ring_of(mesh)
    n = len(ring)
    use_ring = n <= RING_MAX

    def per_device(vectors, rotation, active, factors, owner):
        if use_ring:
            whole = ring_all_gather(rotation, ring).reshape(-1, rotation.shape[1])
        else:
            whole = lax.all_gather(rotation, ("vec", "orb"), axis=0, tiled=True)
        orbitals = whole.shape[0]
        halves = [
            jnp.einsum("sp,sr->pr", whole, v, preferred_element_type=jnp.float32).astype(jnp.bfloat16)
            for v in vectors
        ]
        other_half = jnp.stack([lax.ppermute(h, "orb", [(0, 1), (1, 0)]) for h in halves])
        half_rotated = jnp.stack(halves)

        columns = (active[:, :, None] * B + jnp.arange(B, dtype=jnp.int32)).reshape(
            active.shape[0], -1
        )
        onehot = (
            jnp.arange(orbitals, dtype=jnp.int32)[None, :, None] == columns[:, None, :]
        ).astype(jnp.bfloat16)
        picked = jnp.einsum(
            "rc,gcj->grj", whole, onehot, preferred_element_type=jnp.float32
        ).astype(jnp.bfloat16)
        width = vectors.shape[2]
        first = lax.axis_index("orb") == 0
        lo, hi = picked[:, :width], picked[:, width:]
        mine = jnp.where(first, lo, hi)
        theirs = jnp.where(first, hi, lo)
        active_rotated = (
            jnp.einsum("gpr,grj->gpj", half_rotated, mine, preferred_element_type=jnp.float32)
            + jnp.einsum("gpr,grj->gpj", other_half, theirs, preferred_element_type=jnp.float32)
        ).astype(jnp.bfloat16)

        groups = owner.shape[0]
        group_rows = orbitals // groups
        rows = (owner[:, None] * group_rows + jnp.arange(group_rows, dtype=jnp.int32)).reshape(-1)
        if not use_ring:
            ordered_ar = jnp.take(active_rotated, rows, axis=1)
            ordered = jnp.einsum(
                "gpj,gjq->pq", ordered_ar, factors, preferred_element_type=jnp.float32
            )
            return lax.psum_scatter(ordered, "vec", scatter_dimension=0, tiled=True)

        per = orbitals // n
        held = owner.reshape(n, -1)
        by_group = active_rotated.reshape(active_rotated.shape[0], groups, group_rows, -1)
        me = lax.axis_index("vec")
        reach = n // 2
        back = n - 1 - reach
        shifts = list(range(reach, 0, -1)) + list(range(-back, 0)) + [0]
        even = n % 2 == 0
        table = np.array([[ring[(p + d) % n] for d in shifts] for p in range(n)], np.int32)
        pos_of = np.argsort(np.array(ring))
        by_vec = jnp.asarray(table[pos_of])
        hits = (jnp.arange(n, dtype=jnp.int32) == me)[:, None]
        dest = jnp.sum(jnp.where(hits, by_vec, 0), axis=0)
        order = jnp.sum(
            jnp.where(dest[:, None, None] == jnp.arange(n, dtype=jnp.int32)[None, :, None], held[None], 0),
            axis=1,
        ).reshape(-1)
        ordered = jnp.take(by_group, order, axis=1, mode="clip").reshape(active_rotated.shape)
        part = jnp.einsum(
            "gpj,gjq->pq", ordered, factors, preferred_element_type=jnp.float32
        ).reshape(n, per, -1)
        right = [(ring[i], ring[(i + 1) % n]) for i in range(n)]
        left = [(ring[i], ring[(i - 1) % n]) for i in range(n)]
        if even:
            cut = part.shape[2] // 2
            got_r = lax.ppermute(part[0][:, :cut], "vec", right)
            got_l = lax.ppermute(part[0][:, cut:], "vec", left)
            if reach == 1:
                return part[n - 1] + jnp.concatenate([got_r, got_l], axis=1)
            acc_r = jnp.concatenate([got_r + part[1][:, :cut], part[1][:, cut:]], axis=1)
            acc_l = jnp.concatenate([part[reach][:, :cut], got_l + part[reach][:, cut:]], axis=1)
            for k in range(2, reach):
                acc_r = lax.ppermute(acc_r, "vec", right) + part[k]
                acc_l = lax.ppermute(acc_l, "vec", left) + part[reach + k - 1]
            return (
                part[n - 1]
                + lax.ppermute(acc_r, "vec", right)
                + lax.ppermute(acc_l, "vec", left)
            )
        acc_r = part[0]
        acc_l = part[reach]
        for k in range(1, reach):
            acc_r = lax.ppermute(acc_r, "vec", right) + part[k]
            if k < back:
                acc_l = lax.ppermute(acc_l, "vec", left) + part[reach + k]
        total = part[n - 1] + lax.ppermute(acc_r, "vec", right)
        return total + lax.ppermute(acc_l, "vec", left) if back else total

    return per_device


def solution(mesh):
    placed = (
        P(("grp", "vec"), None, "orb"),
        P(("grp", "vec", "orb"), None),
        P(("grp", "vec"), None),
        P(("grp", "vec"), None, "orb"),
        P("grp"),
    )
    return jax.shard_map(
        make(mesh), mesh=mesh, in_specs=placed, out_specs=P(("grp", "vec"), "orb"), check_vma=False
    )
```

```python
import jax
import jax.numpy as jnp
import numpy as np
from jax import lax
from jax.sharding import PartitionSpec as P

B = 128
RING_MAX = 16


def ring_of(mesh):
    devs = mesh.devices
    n = devs.shape[1]
    coords = [getattr(devs[0, v, 0], "coords", None) for v in range(n)]
    if any(c is None for c in coords):
        return list(range(n))
    zs = sorted({c[2] for c in coords})
    xs = sorted({c[0] for c in coords})
    at = {(c[2], c[0]): v for v, c in enumerate(coords)}
    if len(at) != n or len(zs) * len(xs) != n or len(zs) % 2 or len(xs) < 2:
        return list(range(n))
    cycle = [(z, xs[0]) for z in zs]
    for i, z in enumerate(reversed(zs)):
        row = xs[1:] if i % 2 == 0 else xs[1:][::-1]
        cycle += [(z, x) for x in row]
    return [at[c] for c in cycle]


def swap_orb(x, axis):
    other = lax.ppermute(x, "orb", [(0, 1), (1, 0)])
    first = lax.axis_index("orb") == 0
    lo = jnp.where(first, x, other)
    hi = jnp.where(first, other, x)
    return jnp.concatenate([lo, hi], axis=axis)


def ring_all_gather(x, ring):
    n = len(ring)
    right = [(ring[i], ring[(i + 1) % n]) for i in range(n)]
    left = [(ring[i], ring[(i - 1) % n]) for i in range(n)]
    nr = n // 2
    nl = n - 1 - nr
    rb, lb = [], []
    cur = x
    for _ in range(nr):
        cur = lax.ppermute(cur, "vec", right)
        rb.append(cur)
    cur = x
    for _ in range(nl):
        cur = lax.ppermute(cur, "vec", left)
        lb.append(cur)
    got = [x] + lb + rb[::-1]
    theirs = lax.ppermute(tuple(got), "orb", [(0, 1), (1, 0)])
    pos_of = np.argsort(np.array(ring))
    table = jnp.asarray(((pos_of[None, :] - pos_of[:, None]) % n).astype(np.int32))
    hits = (jnp.arange(n, dtype=jnp.int32) == lax.axis_index("vec"))[:, None]
    offset = jnp.sum(jnp.where(hits, table, 0), axis=0)[:, None, None, None]
    first = lax.axis_index("orb") == 0
    out = jnp.zeros((n, 2) + x.shape, x.dtype)
    for d in range(n):
        pair = jnp.where(first, jnp.stack([got[d], theirs[d]]), jnp.stack([theirs[d], got[d]]))
        out = jnp.where(offset == d, pair[None], out)
    return out


def make(mesh):
    ring = ring_of(mesh)
    n = len(ring)
    use_ring = n <= RING_MAX

    def per_device(vectors, rotation, active, factors, owner):
        if use_ring:
            whole = ring_all_gather(rotation, ring).reshape(-1, rotation.shape[1])
        else:
            whole = lax.all_gather(rotation, ("vec", "orb"), axis=0, tiled=True)
        orbitals = whole.shape[0]
        halves = [
            jnp.einsum("sp,sr->pr", whole, v, preferred_element_type=jnp.float32).astype(jnp.bfloat16)
            for v in vectors
        ]
        other_half = jnp.stack([lax.ppermute(h, "orb", [(0, 1), (1, 0)]) for h in halves])
        half_rotated = jnp.stack(halves)

        columns = (active[:, :, None] * B + jnp.arange(B, dtype=jnp.int32)).reshape(
            active.shape[0], -1
        )
        onehot = (
            jnp.arange(orbitals, dtype=jnp.int32)[None, :, None] == columns[:, None, :]
        ).astype(jnp.bfloat16)
        picked = jnp.einsum(
            "rc,gcj->grj", whole, onehot, preferred_element_type=jnp.float32
        ).astype(jnp.bfloat16)
        width = vectors.shape[2]
        first = lax.axis_index("orb") == 0
        lo, hi = picked[:, :width], picked[:, width:]
        mine = jnp.where(first, lo, hi)
        theirs = jnp.where(first, hi, lo)
        active_rotated = (
            jnp.einsum("gpr,grj->gpj", half_rotated, mine, preferred_element_type=jnp.float32)
            + jnp.einsum("gpr,grj->gpj", other_half, theirs, preferred_element_type=jnp.float32)
        ).astype(jnp.bfloat16)

        groups = owner.shape[0]
        group_rows = orbitals // groups
        rows = (owner[:, None] * group_rows + jnp.arange(group_rows, dtype=jnp.int32)).reshape(-1)
        if not use_ring:
            ordered_ar = jnp.take(active_rotated, rows, axis=1)
            ordered = jnp.einsum(
                "gpj,gjq->pq", ordered_ar, factors, preferred_element_type=jnp.float32
            )
            return lax.psum_scatter(ordered, "vec", scatter_dimension=0, tiled=True)

        per = orbitals // n
        held = owner.reshape(n, -1)
        by_group = active_rotated.reshape(active_rotated.shape[0], groups, group_rows, -1)
        me = lax.axis_index("vec")
        reach = n // 2
        back = n - 1 - reach
        shifts = list(range(reach, 0, -1)) + list(range(-back, 0)) + [0]
        even = n % 2 == 0
        table = np.array([[ring[(p + d) % n] for d in shifts] for p in range(n)], np.int32)
        pos_of = np.argsort(np.array(ring))
        by_vec = jnp.asarray(table[pos_of])
        hits = (jnp.arange(n, dtype=jnp.int32) == me)[:, None]
        dest = jnp.sum(jnp.where(hits, by_vec, 0), axis=0)
        order = jnp.sum(
            jnp.where(dest[:, None, None] == jnp.arange(n, dtype=jnp.int32)[None, :, None], held[None], 0),
            axis=1,
        ).reshape(-1)
        ordered = jnp.take(by_group, order, axis=1, mode="clip").reshape(active_rotated.shape)
        first_block = jnp.einsum(
            "gpj,gjq->pq", ordered[:, :per], factors, preferred_element_type=jnp.float32
        )
        later = ordered[:, per:]
        part = jnp.concatenate(
            [
                first_block[None],
                jnp.einsum(
                    "gpj,gjq->pq", later, factors, preferred_element_type=jnp.float32
                ).reshape(n - 1, per, -1),
            ]
        )
        right = [(ring[i], ring[(i + 1) % n]) for i in range(n)]
        left = [(ring[i], ring[(i - 1) % n]) for i in range(n)]
        if even:
            cut = part.shape[2] // 2
            got_r = lax.ppermute(part[0][:, :cut], "vec", right)
            got_l = lax.ppermute(part[0][:, cut:], "vec", left)
            if reach == 1:
                return part[n - 1] + jnp.concatenate([got_r, got_l], axis=1)
            acc_r = jnp.concatenate([got_r + part[1][:, :cut], part[1][:, cut:]], axis=1)
            acc_l = jnp.concatenate([part[reach][:, :cut], got_l + part[reach][:, cut:]], axis=1)
            for k in range(2, reach):
                acc_r = lax.ppermute(acc_r, "vec", right) + part[k]
                acc_l = lax.ppermute(acc_l, "vec", left) + part[reach + k - 1]
            return (
                part[n - 1]
                + lax.ppermute(acc_r, "vec", right)
                + lax.ppermute(acc_l, "vec", left)
            )
        acc_r = part[0]
        acc_l = part[reach]
        for k in range(1, reach):
            acc_r = lax.ppermute(acc_r, "vec", right) + part[k]
            if k < back:
                acc_l = lax.ppermute(acc_l, "vec", left) + part[reach + k]
        total = part[n - 1] + lax.ppermute(acc_r, "vec", right)
        return total + lax.ppermute(acc_l, "vec", left) if back else total

    return per_device


def solution(mesh):
    placed = (
        P(("grp", "vec"), None, "orb"),
        P(("grp", "vec", "orb"), None),
        P(("grp", "vec"), None),
        P(("grp", "vec"), None, "orb"),
        P("grp"),
    )
    return jax.shard_map(
        make(mesh), mesh=mesh, in_specs=placed, out_specs=P(("grp", "vec"), "orb"), check_vma=False
    )
```
